256 devices in a mesh: leaf: 4 (over x), row: 4 (over y), col: 16 (over z, core).
Axes of the slice: x: 4, y: 4, z: 8, core: 2. Of those that a mesh axis runs over, the one named last changes fastest.
Arguments:
- local_inv: float32 [4, 4, 256, 128, 128], P('leaf', 'row', 'col'), may hold values from -2 to 2, as said below
- local_off: float32 [4, 4, 256, 2, 128, 128], P('leaf', 'row', 'col'), may hold values from -0.09375 to 0.09375
- local_dep: int32 [4, 4, 256, 2], P('leaf', 'row', 'col'), may hold values from 0 to 7
- local_rhs: float32 [4, 4, 256, 64, 128], P('leaf', 'row', 'col'), may hold values from -6 to 6
- top_inv: float32 [8, 4, 16, 128, 128], P(None, 'row', 'col'), may hold values from -2 to 2, as said below
- top_off: float32 [7, 4, 16, 4, 128, 128], P(None, 'row', 'col'), may hold values from -0.125 to 0.125
- top_dep: int32 [7, 4, 16, 4], P(None, 'row', 'col'), may hold values from 0 to 19
- top_rhs: float32 [8, 4, 16, 64, 128], P(None, 'row', 'col'), may hold values from -6 to 6
Outputs:
- local_sol: float32 [4, 4, 256, 64, 128], P('leaf', 'row', 'col')
- top_sol: float32 [8, 4, 16, 64, 128], P(None, 'row', 'col')
The draws below stay inside these ranges and needn't reach their ends.
Inputs may be any that keep to these rules, and one draw needn't show every extreme that they name: `local_inv`: lower-triangular inverse diagonal blocks of a Cholesky factor: entry [t, s] is zero for s > t. `top_inv`: lower-triangular inverse diagonal blocks of a Cholesky factor: entry [t, s] is zero for s > t. `local_dep`: levels of ancestors owned by the supernode's own grid cell. `top_dep`: a value v < 16 names the supernode one level lower in cell (r, v); a value v >= 16 the one in cell (v - 16, c).
All inputs are finite; a program needn't handle non-finite values.
Results may differ from the reference program's by a relative error of at most 0.0001.
Values sent between devices are 32-bit elements; how exact they have to be, the bound alone decides.
No kernel may reach another device: no remote copies, remote signals or barrier semaphores. Data moves between devices by JAX's collectives and lax.ppermute only.
A program may use at most 64 MiB of HBM per device.

```python
import jax
import jax.numpy as jnp
from jax import lax

S = 128
R = 64
LOC = 16
FAN = 2
DEP = 4
LEVELS = 8
N_LEAF = 4
N_ROW = 4
N_COL = 16


def inverse_blocks(key, shape):
    key_off, key_diag = jax.random.split(key)
    identity = jnp.eye(S, dtype=jnp.float32)
    lower = (jnp.arange(S)[:, None] > jnp.arange(S)[None, :]).astype(jnp.float32)
    spread = jax.random.normal(key_off, shape, jnp.float32) * (0.8 / S ** 0.5)
    diagonal = jax.random.uniform(key_diag, shape[:-1], jnp.float32, 0.5, 1.5)
    return spread * lower + diagonal[..., None] * identity


def draw_local_inv(key, part):
    return inverse_blocks(jax.random.fold_in(key, 11), (N_LEAF, N_ROW, N_COL * LOC, S, S))


def draw_top_inv(key, part):
    return inverse_blocks(jax.random.fold_in(key, 23), (LEVELS, N_ROW, N_COL, S, S))


def plant(values, rng, low, top_value):
    dims = values.shape
    spot = [jax.random.randint(jax.random.fold_in(rng, axis), (), 0, dims[axis]) for axis in range(len(dims))]
    values = values.at[tuple(spot)].set(low)
    longest = dims.index(max(dims))
    spot[longest] = (spot[longest] + 1) % dims[longest]
    return values.at[tuple(spot)].set(top_value)


def block_levels(rng, shape, shards, smallest, top_value):
    factor_of, own = 1.0, jax.random.fold_in(rng, 6)
    for axis_at, parts in shards:
        steps = jnp.exp(jax.random.uniform(jax.random.fold_in(own, axis_at), (parts,), jnp.float32, smallest / len(shards), top_value / len(shards)))
        factor_of = factor_of * jnp.repeat(steps, shape[axis_at] // parts).reshape([-1 if axis == axis_at else 1 for axis in range(len(shape))])
    return factor_of


def scatter_about(rng, dims, scale, reach, cuts=(), held_as=jnp.bfloat16):
    array = scale * jax.random.normal(rng, dims, jnp.float32)
    if cuts:
        array = array * block_levels(rng, dims, cuts, -0.22, 0.18)
    return jnp.clip(array, -reach, reach).astype(held_as)


def setup_inputs(seed: int = 0) -> dict:
    keys = jax.random.split(jax.random.key(seed), 9)
    local_inv = draw_local_inv(jax.random.fold_in(keys[8], 71), 0)
    local_off = scatter_about(keys[1], (N_LEAF, N_ROW, N_COL * LOC, FAN, S, S), (S * LOC * FAN) ** -0.5, 0.09375, ((0, 4), (1, 4), (2, 16)), jnp.float32)
    local_dep = plant(jax.random.randint(keys[2], (N_LEAF, N_ROW, N_COL * LOC, FAN), 0, LEVELS), jax.random.fold_in(keys[2], 1), 0, LEVELS - 1).astype(jnp.int32)
    local_rhs = scatter_about(keys[3], (N_LEAF, N_ROW, N_COL * LOC, R, S), 1.0, 6.0, ((0, 4), (1, 4), (2, 16)), jnp.float32)
    top_inv = draw_top_inv(jax.random.fold_in(keys[8], 71), 0)
    top_off = scatter_about(keys[5], (LEVELS - 1, N_ROW, N_COL, DEP, S, S), (4 * DEP * S) ** -0.5, 0.125, ((1, 4), (2, 16)), jnp.float32)
    top_dep = plant(jax.random.randint(keys[6], (LEVELS - 1, N_ROW, N_COL, DEP), 0, N_COL + N_ROW), jax.random.fold_in(keys[6], 1), 0, (N_COL + N_ROW) - 1).astype(jnp.int32)
    top_rhs = scatter_about(keys[7], (LEVELS, N_ROW, N_COL, R, S), 1.0, 6.0, ((1, 4), (2, 16)), jnp.float32)
    return dict(local_inv=local_inv, local_off=local_off, local_dep=local_dep, local_rhs=local_rhs, top_inv=top_inv, top_off=top_off, top_dep=top_dep, top_rhs=top_rhs)


highest = lax.Precision.HIGHEST


def reference(local_inv, local_off, local_dep, local_rhs, top_inv, top_off, top_dep, top_rhs):
    inverse = local_inv.reshape(N_LEAF, N_ROW, N_COL, LOC, S, S)
    blocks = local_off.reshape(N_LEAF, N_ROW, N_COL, LOC, FAN, S, S)
    ancestor_levels = local_dep.reshape(N_LEAF, N_ROW, N_COL, LOC, FAN)
    right_local = local_rhs.reshape(N_LEAF, N_ROW, N_COL, LOC, R, S)
    local_first = jnp.einsum('abckrs,abckts->abckrt', right_local, inverse, precision=highest)
    matches = (ancestor_levels[..., None] == jnp.arange(LEVELS, dtype=jnp.int32)).astype(jnp.float32)
    contributions = jnp.einsum('abckrs,abckjts->abckjrt', local_first, blocks, precision=highest)
    updates = jnp.einsum('abckjl,abckjrt->lbcrt', matches, contributions, precision=highest)
    forward = []
    for height in range(LEVELS):
        target = top_rhs[height] - updates[height]
        if height > 0:
            latest = forward[-1]
            cand_cols = jnp.broadcast_to(latest[:, None], (N_ROW, N_COL, N_COL, R, S))
            cand_rows = jnp.broadcast_to(jnp.transpose(latest, (1, 0, 2, 3))[None], (N_ROW, N_COL, N_ROW, R, S))
            candidates = jnp.concatenate([cand_cols, cand_rows], axis=2)
            picks = (top_dep[height - 1][..., None] == jnp.arange(N_COL + N_ROW, dtype=jnp.int32)).astype(jnp.float32)
            picked = jnp.einsum('abjv,abvrs->abjrs', picks, candidates, precision=highest)
            target = target - jnp.einsum('abjrs,abjts->abrt', picked, top_off[height - 1], precision=highest)
        forward.append(jnp.einsum('abrs,abts->abrt', target, top_inv[height], precision=highest))
    backward = [None] * LEVELS
    current = jnp.einsum('abrs,abst->abrt', forward[LEVELS - 1], top_inv[LEVELS - 1], precision=highest)
    backward[LEVELS - 1] = current
    for height in range(LEVELS - 2, -1, -1):
        pieces = jnp.einsum('abrt,abjts->abjrs', current, top_off[height], precision=highest)
        sources = top_dep[height]
        to_cols = (sources[..., None] == jnp.arange(N_COL, dtype=jnp.int32)).astype(jnp.float32)
        to_rows = (sources[..., None] == N_COL + jnp.arange(N_ROW, dtype=jnp.int32)).astype(jnp.float32)
        incoming = jnp.einsum('abjv,abjrs->avrs', to_cols, pieces, precision=highest)
        incoming = incoming + jnp.einsum('abju,abjrs->ubrs', to_rows, pieces, precision=highest)
        current = jnp.einsum('abrs,abst->abrt', forward[height] - incoming, top_inv[height], precision=highest)
        backward[height] = current
    top_solution = jnp.stack(backward)
    ancestors = jnp.einsum('abckjl,lbcrt->abckjrt', matches, top_solution, precision=highest)
    remainder = local_first - jnp.einsum('abckjrt,abckjts->abckrs', ancestors, blocks, precision=highest)
    local_solution = jnp.einsum('abckrs,abckst->abckrt', remainder, inverse, precision=highest)
    return local_solution.reshape(N_LEAF, N_ROW, N_COL * LOC, R, S), top_solution
```

```python
import jax
import jax.numpy as jnp
from jax import lax
from jax.sharding import PartitionSpec as P

highest = lax.Precision.HIGHEST


def apply_inverse(inverse, block):
    return jnp.einsum("rs,ts->rt", block, inverse, precision=highest)


def apply_transpose(inverse, block):
    return jnp.einsum("rs,st->rt", block, inverse, precision=highest)


def shifted(value, axis, k):
    n = lax.axis_size(axis)
    return lax.ppermute(value, axis, [(i, (i + k) % n) for i in range(n)])


def gather_sources(block, sources, width_cols):
    by_col = lax.all_gather(block[None], "col", axis=0, tiled=True)
    n_row = lax.axis_size("row")
    me_row = lax.axis_index("row")
    by_shift = [block] + [shifted(block, "row", k) for k in range(1, n_row)]
    picked = []
    for j in range(sources.shape[0]):
        v = sources[j]
        from_col = lax.dynamic_index_in_dim(by_col, jnp.clip(v, 0, width_cols - 1), 0, keepdims=False)
        need = (me_row - (v - width_cols)) % n_row
        from_row = by_shift[0]
        for k in range(1, n_row):
            from_row = jnp.where(need == k, by_shift[k], from_row)
        picked.append(jnp.where(v < width_cols, from_col, from_row))
    return jnp.stack(picked)


def push_back(pieces, sources, width_cols):
    n_row = lax.axis_size("row")
    me_row = lax.axis_index("row")
    zero = jnp.zeros_like(pieces[0])
    slots = jnp.stack(
        [
            sum(jnp.where(sources[j] == v, pieces[j], zero) for j in range(pieces.shape[0]))
            for v in range(width_cols)
        ]
    )
    from_cols = lax.all_to_all(slots, "col", 0, 0, tiled=True).sum(0)
    shift_of = (sources - width_cols - me_row) % n_row
    incoming = from_cols
    for k in range(n_row):
        part = sum(
            jnp.where((sources[j] >= width_cols) & (shift_of[j] == k), pieces[j], zero)
            for j in range(pieces.shape[0])
        )
        incoming = incoming + (part if k == 0 else shifted(part, "row", k))
    return incoming


def solve_top(top_inverse, top_blocks, top_links, top_right, updates):
    levels = top_inverse.shape[0]
    width_cols = lax.axis_size("col")
    forward = []
    for height in range(levels):
        target = top_right[height] - updates[height]
        if height > 0:
            picked = gather_sources(forward[-1], top_links[height - 1], width_cols)
            target = target - jnp.einsum(
                "jrs,jts->rt", picked, top_blocks[height - 1], precision=highest
            )
        forward.append(apply_inverse(top_inverse[height], target))
    backward = [None] * levels
    current = apply_transpose(top_inverse[levels - 1], forward[levels - 1])
    backward[levels - 1] = current
    for height in range(levels - 2, -1, -1):
        pieces = jnp.einsum("rt,jts->jrs", current, top_blocks[height], precision=highest)
        incoming = push_back(pieces, top_links[height], width_cols)
        current = apply_transpose(top_inverse[height], forward[height] - incoming)
        backward[height] = current
    return jnp.stack(backward)


def on_device(local_inv, local_off, local_dep, local_rhs, top_inv, top_off, top_dep, top_rhs):
    inverse = local_inv[0, 0]
    blocks = local_off[0, 0]
    ancestor_levels = local_dep[0, 0]
    right_local = local_rhs[0, 0]
    levels = top_inv.shape[0]
    top_inverse = top_inv[:, 0, 0]
    top_blocks = top_off[:, 0, 0]
    top_links = top_dep[:, 0, 0]
    top_right = top_rhs[:, 0, 0]
    local_first = jnp.einsum("krs,kts->krt", right_local, inverse, precision=highest)
    contributions = jnp.einsum("krs,kjts->kjrt", local_first, blocks, precision=highest)
    level_matches = (ancestor_levels[:, :, None] == jnp.arange(levels, dtype=jnp.int32)).astype(
        jnp.float32
    )
    updates = jnp.einsum("kjl,kjrt->lrt", level_matches, contributions, precision=highest)
    n_leaf = lax.axis_size("leaf")
    me_leaf = lax.axis_index("leaf")
    by_shift = [updates] + [shifted(updates, "leaf", k) for k in range(1, n_leaf)]
    totals = None
    for u in range(n_leaf):
        shift = (me_leaf - u) % n_leaf
        term = by_shift[0]
        for k in range(1, n_leaf):
            term = jnp.where(shift == k, by_shift[k], term)
        totals = term if totals is None else totals + term
    top_solution = solve_top(top_inverse, top_blocks, top_links, top_right, totals)
    ancestors = jnp.einsum("kjl,lrt->kjrt", level_matches, top_solution, precision=highest)
    remainder = local_first - jnp.einsum("kjrt,kjts->krs", ancestors, blocks, precision=highest)
    local_solution = jnp.einsum("krs,kst->krt", remainder, inverse, precision=highest)
    return (local_solution[None, None], top_solution[:, None, None])


def solution(mesh):
    placed = (
        P("leaf", "row", "col", None, None),
        P("leaf", "row", "col", None, None, None),
        P("leaf", "row", "col", None),
        P("leaf", "row", "col", None, None),
        P(None, "row", "col", None, None),
        P(None, "row", "col", None, None, None),
        P(None, "row", "col", None),
        P(None, "row", "col", None, None),
    )
    return jax.shard_map(
        on_device,
        mesh=mesh,
        in_specs=placed,
        out_specs=(P("leaf", "row", "col", None, None), P(None, "row", "col", None, None)),
        check_vma=False,
    )
```

```python
import jax
import jax.numpy as jnp
from jax import lax
from jax.sharding import PartitionSpec as P

highest = lax.Precision.HIGHEST


def apply_inverse(inverse, block):
    return jnp.einsum("rs,ts->rt", block, inverse, precision=highest)


def apply_transpose(inverse, block):
    return jnp.einsum("rs,st->rt", block, inverse, precision=highest)


def shifted(value, axis, k):
    n = lax.axis_size(axis)
    return lax.ppermute(value, axis, [(i, (i + k) % n) for i in range(n)])


def gather_sources(block, sources, width_cols):
    by_col = lax.all_gather(block[None], "col", axis=0, tiled=True)
    n_row = lax.axis_size("row")
    me_row = lax.axis_index("row")
    by_shift = [block] + [shifted(block, "row", k) for k in range(1, n_row)]
    picked = []
    for j in range(sources.shape[0]):
        v = sources[j]
        from_col = lax.dynamic_index_in_dim(by_col, jnp.clip(v, 0, width_cols - 1), 0, keepdims=False)
        need = (me_row - (v - width_cols)) % n_row
        from_row = by_shift[0]
        for k in range(1, n_row):
            from_row = jnp.where(need == k, by_shift[k], from_row)
        picked.append(jnp.where(v < width_cols, from_col, from_row))
    return jnp.stack(picked)


def push_back(pieces, sources, width_cols):
    n_row = lax.axis_size("row")
    me_row = lax.axis_index("row")
    zero = jnp.zeros_like(pieces[0])
    slots = jnp.stack(
        [
            sum(jnp.where(sources[j] == v, pieces[j], zero) for j in range(pieces.shape[0]))
            for v in range(width_cols)
        ]
    )
    from_cols = lax.all_to_all(slots, "col", 0, 0, tiled=True).sum(0)
    shift_of = (sources - width_cols - me_row) % n_row
    incoming = from_cols
    for k in range(n_row):
        part = sum(
            jnp.where((sources[j] >= width_cols) & (shift_of[j] == k), pieces[j], zero)
            for j in range(pieces.shape[0])
        )
        incoming = incoming + (part if k == 0 else shifted(part, "row", k))
    return incoming


def solve_top(top_inverse, top_blocks, top_links, top_right, updates):
    levels = top_inverse.shape[0]
    width_cols = lax.axis_size("col")
    forward = []
    for height in range(levels):
        target = top_right[height] - updates[height]
        if height > 0:
            picked = gather_sources(forward[-1], top_links[height - 1], width_cols)
            target = target - jnp.einsum(
                "jrs,jts->rt", picked, top_blocks[height - 1], precision=highest
            )
        forward.append(apply_inverse(top_inverse[height], target))
    backward = [None] * levels
    current = apply_transpose(top_inverse[levels - 1], forward[levels - 1])
    backward[levels - 1] = current
    for height in range(levels - 2, -1, -1):
        pieces = jnp.einsum("rt,jts->jrs", current, top_blocks[height], precision=highest)
        incoming = push_back(pieces, top_links[height], width_cols)
        current = apply_transpose(top_inverse[height], forward[height] - incoming)
        backward[height] = current
    return jnp.stack(backward)


def on_device(local_inv, local_off, local_dep, local_rhs, top_inv, top_off, top_dep, top_rhs):
    inverse = local_inv[0, 0]
    blocks = local_off[0, 0]
    ancestor_levels = local_dep[0, 0]
    right_local = local_rhs[0, 0]
    levels = top_inv.shape[0]
    top_inverse = top_inv[:, 0, 0]
    top_blocks = top_off[:, 0, 0]
    top_links = top_dep[:, 0, 0]
    top_right = top_rhs[:, 0, 0]
    local_first = jnp.einsum("krs,kts->krt", right_local, inverse, precision=highest)
    contributions = jnp.einsum("krs,kjts->kjrt", local_first, blocks, precision=highest)
    level_matches = (ancestor_levels[:, :, None] == jnp.arange(levels, dtype=jnp.int32)).astype(
        jnp.float32
    )
    updates = jnp.einsum("kjl,kjrt->lrt", level_matches, contributions, precision=highest)
    n_leaf = lax.axis_size("leaf")
    me_leaf = lax.axis_index("leaf")
    first = updates[0]
    by_shift = [first] + [shifted(first, "leaf", k) for k in range(1, n_leaf)]
    total_first = None
    for u in range(n_leaf):
        shift = (me_leaf - u) % n_leaf
        term = by_shift[0]
        for k in range(1, n_leaf):
            term = jnp.where(shift == k, by_shift[k], term)
        total_first = term if total_first is None else total_first + term
    rest = lax.psum(updates[1:], "leaf")
    totals = [total_first] + [rest[i] for i in range(levels - 1)]
    top_solution = solve_top(top_inverse, top_blocks, top_links, top_right, totals)
    ancestors = jnp.einsum("kjl,lrt->kjrt", level_matches, top_solution, precision=highest)
    remainder = local_first - jnp.einsum("kjrt,kjts->krs", ancestors, blocks, precision=highest)
    local_solution = jnp.einsum("krs,kst->krt", remainder, inverse, precision=highest)
    return (local_solution[None, None], top_solution[:, None, None])


def solution(mesh):
    placed = (
        P("leaf", "row", "col", None, None),
        P("leaf", "row", "col", None, None, None),
        P("leaf", "row", "col", None),
        P("leaf", "row", "col", None, None),
        P(None, "row", "col", None, None),
        P(None, "row", "col", None, None, None),
        P(None, "row", "col", None),
        P(None, "row", "col", None, None),
    )
    return jax.shard_map(
        on_device,
        mesh=mesh,
        in_specs=placed,
        out_specs=(P("leaf", "row", "col", None, None), P(None, "row", "col", None, None)),
        check_vma=False,
    )
```

```python
import jax
import jax.numpy as jnp
from jax import lax
from jax.sharding import PartitionSpec as P

highest = lax.Precision.HIGHEST


def apply_inverse(inverse, block):
    return jnp.einsum("rs,ts->rt", block, inverse, precision=highest)


def apply_transpose(inverse, block):
    return jnp.einsum("rs,st->rt", block, inverse, precision=highest)


def shifted(value, axis, k):
    n = lax.axis_size(axis)
    return lax.ppermute(value, axis, [(i, (i + k) % n) for i in range(n)])


def gather_sources(block, sources, width_cols):
    by_col = lax.all_gather(block[None], "col", axis=0, tiled=True)
    n_row = lax.axis_size("row")
    me_row = lax.axis_index("row")
    by_shift = [block] + [shifted(block, "row", k) for k in range(1, n_row)]
    picked = []
    for j in range(sources.shape[0]):
        v = sources[j]
        from_col = lax.dynamic_index_in_dim(by_col, jnp.clip(v, 0, width_cols - 1), 0, keepdims=False)
        need = (me_row - (v - width_cols)) % n_row
        from_row = by_shift[0]
        for k in range(1, n_row):
            from_row = jnp.where(need == k, by_shift[k], from_row)
        picked.append(jnp.where(v < width_cols, from_col, from_row))
    return jnp.stack(picked)


def push_back(pieces, sources, width_cols):
    n_row = lax.axis_size("row")
    me_row = lax.axis_index("row")
    zero = jnp.zeros_like(pieces[0])
    slots = jnp.stack(
        [
            sum(jnp.where(sources[j] == v, pieces[j], zero) for j in range(pieces.shape[0]))
            for v in range(width_cols)
        ]
    )
    from_cols = lax.all_to_all(slots, "col", 0, 0, tiled=True).sum(0)
    shift_of = (sources - width_cols - me_row) % n_row
    incoming = from_cols
    for k in range(n_row):
        part = sum(
            jnp.where((sources[j] >= width_cols) & (shift_of[j] == k), pieces[j], zero)
            for j in range(pieces.shape[0])
        )
        incoming = incoming + (part if k == 0 else shifted(part, "row", k))
    return incoming


def solve_top(top_inverse, top_blocks, top_links, top_right, updates):
    levels = top_inverse.shape[0]
    width_cols = lax.axis_size("col")
    forward = []
    for height in range(levels):
        target = top_right[height] - updates[height]
        if height > 0:
            picked = gather_sources(forward[-1], top_links[height - 1], width_cols)
            target = target - jnp.einsum(
                "jrs,jts->rt", picked, top_blocks[height - 1], precision=highest
            )
        forward.append(apply_inverse(top_inverse[height], target))
    backward = [None] * levels
    current = apply_transpose(top_inverse[levels - 1], forward[levels - 1])
    backward[levels - 1] = current
    for height in range(levels - 2, -1, -1):
        pieces = jnp.einsum("rt,jts->jrs", current, top_blocks[height], precision=highest)
        incoming = push_back(pieces, top_links[height], width_cols)
        current = apply_transpose(top_inverse[height], forward[height] - incoming)
        backward[height] = current
    return jnp.stack(backward)


def on_device(local_inv, local_off, local_dep, local_rhs, top_inv, top_off, top_dep, top_rhs):
    inverse = local_inv[0, 0]
    blocks = local_off[0, 0]
    ancestor_levels = local_dep[0, 0]
    right_local = local_rhs[0, 0]
    levels = top_inv.shape[0]
    top_inverse = top_inv[:, 0, 0]
    top_blocks = top_off[:, 0, 0]
    top_links = top_dep[:, 0, 0]
    top_right = top_rhs[:, 0, 0]
    local_first = jnp.einsum("krs,kts->krt", right_local, inverse, precision=highest)
    contributions = jnp.einsum("krs,kjts->kjrt", local_first, blocks, precision=highest)
    level_matches = (ancestor_levels[:, :, None] == jnp.arange(levels, dtype=jnp.int32)).astype(
        jnp.float32
    )
    updates = jnp.einsum("kjl,kjrt->lrt", level_matches, contributions, precision=highest)
    totals = lax.psum(updates, "leaf")
    top_solution = solve_top(top_inverse, top_blocks, top_links, top_right, totals)
    ancestors = jnp.einsum("kjl,lrt->kjrt", level_matches, top_solution, precision=highest)
    remainder = local_first - jnp.einsum("kjrt,kjts->krs", ancestors, blocks, precision=highest)
    local_solution = jnp.einsum("krs,kst->krt", remainder, inverse, precision=highest)
    return (local_solution[None, None], top_solution[:, None, None])


def solution(mesh):
    placed = (
        P("leaf", "row", "col", None, None),
        P("leaf", "row", "col", None, None, None),
        P("leaf", "row", "col", None),
        P("leaf", "row", "col", None, None),
        P(None, "row", "col", None, None),
        P(None, "row", "col", None, None, None),
        P(None, "row", "col", None),
        P(None, "row", "col", None, None),
    )
    return jax.shard_map(
        on_device,
        mesh=mesh,
        in_specs=placed,
        out_specs=(P("leaf", "row", "col", None, None), P(None, "row", "col", None, None)),
        check_vma=False,
    )
```

```python
import jax
import jax.numpy as jnp
from jax import lax
from jax.sharding import PartitionSpec as P

highest = lax.Precision.HIGHEST


def apply_inverse(inverse, block):
    return jnp.einsum("rs,ts->rt", block, inverse, precision=highest)


def apply_transpose(inverse, block):
    return jnp.einsum("rs,st->rt", block, inverse, precision=highest)


def shifted(value, axis, k):
    n = lax.axis_size(axis)
    return lax.ppermute(value, axis, [(i, (i + k) % n) for i in range(n)])


def gather_sources(block, col_pick, row_pick):
    by_col = lax.all_gather(block[None], "col", axis=0, tiled=True)
    n_row = lax.axis_size("row")
    by_shift = jnp.stack([block] + [shifted(block, "row", k) for k in range(1, n_row)])
    return jnp.einsum("jv,vrs->jrs", col_pick, by_col, precision=highest) + jnp.einsum(
        "jk,krs->jrs", row_pick, by_shift, precision=highest
    )


def push_back(pieces, col_pick, row_push):
    n_row = lax.axis_size("row")
    slots = jnp.einsum("jv,jrs->vrs", col_pick, pieces, precision=highest)
    incoming = lax.all_to_all(slots, "col", 0, 0, tiled=True).sum(0)
    parts = jnp.einsum("jk,jrs->krs", row_push, pieces, precision=highest)
    incoming = incoming + parts[0]
    for k in range(1, n_row):
        incoming = incoming + shifted(parts[k], "row", k)
    return incoming


def solve_top(top_inverse, top_blocks, top_links, top_right, updates):
    levels = top_inverse.shape[0]
    width_cols = lax.axis_size("col")
    n_row = lax.axis_size("row")
    me_row = lax.axis_index("row")
    is_col = top_links < width_cols
    col_pick = (top_links[..., None] == jnp.arange(width_cols, dtype=jnp.int32)).astype(jnp.float32)
    pull = jnp.mod(me_row - (top_links - width_cols), n_row)
    push = jnp.mod(top_links - width_cols - me_row, n_row)
    shifts = jnp.arange(n_row, dtype=jnp.int32)
    row_pick = ((~is_col)[..., None] & (pull[..., None] == shifts)).astype(jnp.float32)
    row_push = ((~is_col)[..., None] & (push[..., None] == shifts)).astype(jnp.float32)
    forward = []
    for height in range(levels):
        target = top_right[height] - updates[height]
        if height > 0:
            picked = gather_sources(forward[-1], col_pick[height - 1], row_pick[height - 1])
            target = target - jnp.einsum(
                "jrs,jts->rt", picked, top_blocks[height - 1], precision=highest
            )
        forward.append(apply_inverse(top_inverse[height], target))
    backward = [None] * levels
    current = apply_transpose(top_inverse[levels - 1], forward[levels - 1])
    backward[levels - 1] = current
    for height in range(levels - 2, -1, -1):
        pieces = jnp.einsum("rt,jts->jrs", current, top_blocks[height], precision=highest)
        incoming = push_back(pieces, col_pick[height], row_push[height])
        current = apply_transpose(top_inverse[height], forward[height] - incoming)
        backward[height] = current
    return jnp.stack(backward)


def on_device(local_inv, local_off, local_dep, local_rhs, top_inv, top_off, top_dep, top_rhs):
    inverse = local_inv[0, 0]
    blocks = local_off[0, 0]
    ancestor_levels = local_dep[0, 0]
    right_local = local_rhs[0, 0]
    levels = top_inv.shape[0]
    top_inverse = top_inv[:, 0, 0]
    top_blocks = top_off[:, 0, 0]
    top_links = top_dep[:, 0, 0]
    top_right = top_rhs[:, 0, 0]
    local_first = jnp.einsum("krs,kts->krt", right_local, inverse, precision=highest)
    contributions = jnp.einsum("krs,kjts->kjrt", local_first, blocks, precision=highest)
    level_matches = (ancestor_levels[:, :, None] == jnp.arange(levels, dtype=jnp.int32)).astype(
        jnp.float32
    )
    updates = jnp.einsum("kjl,kjrt->lrt", level_matches, contributions, precision=highest)
    totals = lax.psum(updates, "leaf")
    top_solution = solve_top(top_inverse, top_blocks, top_links, top_right, totals)
    ancestors = jnp.einsum("kjl,lrt->kjrt", level_matches, top_solution, precision=highest)
    remainder = local_first - jnp.einsum("kjrt,kjts->krs", ancestors, blocks, precision=highest)
    local_solution = jnp.einsum("krs,kst->krt", remainder, inverse, precision=highest)
    return (local_solution[None, None], top_solution[:, None, None])


def solution(mesh):
    placed = (
        P("leaf", "row", "col", None, None),
        P("leaf", "row", "col", None, None, None),
        P("leaf", "row", "col", None),
        P("leaf", "row", "col", None, None),
        P(None, "row", "col", None, None),
        P(None, "row", "col", None, None, None),
        P(None, "row", "col", None),
        P(None, "row", "col", None, None),
    )
    return jax.shard_map(
        on_device,
        mesh=mesh,
        in_specs=placed,
        out_specs=(P("leaf", "row", "col", None, None), P(None, "row", "col", None, None)),
        check_vma=False,
    )
```

```python
import jax
import jax.numpy as jnp
from jax import lax
from jax.sharding import PartitionSpec as P

highest = lax.Precision.HIGHEST


def apply_inverse(inverse, block):
    return jnp.einsum("rs,ts->rt", block, inverse, precision=highest)


def apply_transpose(inverse, block):
    return jnp.einsum("rs,st->rt", block, inverse, precision=highest)


def shifted(value, axis, k):
    n = lax.axis_size(axis)
    return lax.ppermute(value, axis, [(i, (i + k) % n) for i in range(n)])


def gather_sources(block, col_pick, row_pick):
    by_col = lax.all_gather(block[None], "col", axis=0, tiled=True)
    n_row = lax.axis_size("row")
    by_shift = jnp.stack([block] + [shifted(block, "row", k) for k in range(1, n_row)])
    return jnp.einsum("jv,vrs->jrs", col_pick, by_col, precision=highest) + jnp.einsum(
        "jk,krs->jrs", row_pick, by_shift, precision=highest
    )


def push_back(pieces, col_pick, row_push):
    n_row = lax.axis_size("row")
    slots = jnp.einsum("jv,jrs->vrs", col_pick, pieces, precision=highest)
    incoming = lax.all_to_all(slots, "col", 0, 0, tiled=True).sum(0)
    parts = jnp.einsum("jk,jrs->krs", row_push, pieces, precision=highest)
    incoming = incoming + parts[0]
    for k in range(1, n_row):
        incoming = incoming + shifted(parts[k], "row", k)
    return incoming


def solve_top(top_inverse, top_blocks, top_links, top_right, updates):
    levels = top_inverse.shape[0]
    width_cols = lax.axis_size("col")
    n_row = lax.axis_size("row")
    me_row = lax.axis_index("row")
    is_col = top_links < width_cols
    col_pick = (top_links[..., None] == jnp.arange(width_cols, dtype=jnp.int32)).astype(jnp.float32)
    pull = jnp.mod(me_row - (top_links - width_cols), n_row)
    push = jnp.mod(top_links - width_cols - me_row, n_row)
    shifts = jnp.arange(n_row, dtype=jnp.int32)
    row_pick = ((~is_col)[..., None] & (pull[..., None] == shifts)).astype(jnp.float32)
    row_push = ((~is_col)[..., None] & (push[..., None] == shifts)).astype(jnp.float32)
    forward = []
    for height in range(levels):
        target = top_right[height] - updates[height]
        if height > 0:
            picked = gather_sources(forward[-1], col_pick[height - 1], row_pick[height - 1])
            target = target - jnp.einsum(
                "jrs,jts->rt", picked, top_blocks[height - 1], precision=highest
            )
        forward.append(apply_inverse(top_inverse[height], target))
    backward = [None] * levels
    current = apply_transpose(top_inverse[levels - 1], forward[levels - 1])
    backward[levels - 1] = current
    for height in range(levels - 2, -1, -1):
        pieces = jnp.einsum("rt,jts->jrs", current, top_blocks[height], precision=highest)
        incoming = push_back(pieces, col_pick[height], row_push[height])
        current = apply_transpose(top_inverse[height], forward[height] - incoming)
        backward[height] = current
    return jnp.stack(backward)


def on_device(local_inv, local_off, local_dep, local_rhs, top_inv, top_off, top_dep, top_rhs):
    inverse = local_inv[0, 0]
    blocks = local_off[0, 0]
    ancestor_levels = local_dep[0, 0]
    right_local = local_rhs[0, 0]
    levels = top_inv.shape[0]
    top_inverse = top_inv[:, 0, 0]
    top_blocks = top_off[:, 0, 0]
    top_links = top_dep[:, 0, 0]
    top_right = top_rhs[:, 0, 0]
    local_first = jnp.einsum("krs,kts->krt", right_local, inverse, precision=highest)
    contributions = jnp.einsum("krs,kjts->kjrt", local_first, blocks, precision=highest)
    level_matches = (ancestor_levels[:, :, None] == jnp.arange(levels, dtype=jnp.int32)).astype(
        jnp.float32
    )
    updates = jnp.einsum("kjl,kjrt->lrt", level_matches, contributions, precision=highest)
    n_leaf = lax.axis_size("leaf")
    by_shift = jnp.stack([updates] + [shifted(updates, "leaf", k) for k in range(1, n_leaf)])
    order = jnp.mod(lax.axis_index("leaf") - jnp.arange(n_leaf, dtype=jnp.int32), n_leaf)
    weights = (order[:, None] == jnp.arange(n_leaf, dtype=jnp.int32)).astype(jnp.float32)
    ordered = jnp.einsum("uk,klrs->ulrs", weights, by_shift, precision=highest)
    totals = ordered[0]
    for u in range(1, n_leaf):
        totals = totals + ordered[u]
    top_solution = solve_top(top_inverse, top_blocks, top_links, top_right, totals)
    ancestors = jnp.einsum("kjl,lrt->kjrt", level_matches, top_solution, precision=highest)
    remainder = local_first - jnp.einsum("kjrt,kjts->krs", ancestors, blocks, precision=highest)
    local_solution = jnp.einsum("krs,kst->krt", remainder, inverse, precision=highest)
    return (local_solution[None, None], top_solution[:, None, None])


def solution(mesh):
    placed = (
        P("leaf", "row", "col", None, None),
        P("leaf", "row", "col", None, None, None),
        P("leaf", "row", "col", None),
        P("leaf", "row", "col", None, None),
        P(None, "row", "col", None, None),
        P(None, "row", "col", None, None, None),
        P(None, "row", "col", None),
        P(None, "row", "col", None, None),
    )
    return jax.shard_map(
        on_device,
        mesh=mesh,
        in_specs=placed,
        out_specs=(P("leaf", "row", "col", None, None), P(None, "row", "col", None, None)),
        check_vma=False,
    )
```

```python
import jax
import jax.numpy as jnp
from jax import lax
from jax.sharding import PartitionSpec as P

highest = lax.Precision.HIGHEST


def apply_inverse(inverse, block):
    return jnp.einsum("rs,ts->rt", block, inverse, precision=highest)


def apply_transpose(inverse, block):
    return jnp.einsum("rs,st->rt", block, inverse, precision=highest)


def shifted(value, axis, k):
    n = lax.axis_size(axis)
    return lax.ppermute(value, axis, [(i, (i + k) % n) for i in range(n)])


def gather_sources(block, col_pick, row_pick):
    width_cols = lax.axis_size("col")
    by_col = lax.all_to_all(
        jnp.broadcast_to(block[None], (width_cols,) + block.shape), "col", 0, 0, tiled=True
    )
    n_row = lax.axis_size("row")
    by_shift = jnp.stack([block] + [shifted(block, "row", k) for k in range(1, n_row)])
    return jnp.einsum("jv,vrs->jrs", col_pick, by_col, precision=highest) + jnp.einsum(
        "jk,krs->jrs", row_pick, by_shift, precision=highest
    )


def push_back(pieces, col_pick, row_push):
    n_row = lax.axis_size("row")
    slots = jnp.einsum("jv,jrs->vrs", col_pick, pieces, precision=highest)
    incoming = lax.all_to_all(slots, "col", 0, 0, tiled=True).sum(0)
    parts = jnp.einsum("jk,jrs->krs", row_push, pieces, precision=highest)
    incoming = incoming + parts[0]
    for k in range(1, n_row):
        incoming = incoming + shifted(parts[k], "row", k)
    return incoming


def solve_top(top_inverse, top_blocks, top_links, top_right, updates):
    levels = top_inverse.shape[0]
    width_cols = lax.axis_size("col")
    n_row = lax.axis_size("row")
    me_row = lax.axis_index("row")
    is_col = top_links < width_cols
    col_pick = (top_links[..., None] == jnp.arange(width_cols, dtype=jnp.int32)).astype(jnp.float32)
    pull = jnp.mod(me_row - (top_links - width_cols), n_row)
    push = jnp.mod(top_links - width_cols - me_row, n_row)
    shifts = jnp.arange(n_row, dtype=jnp.int32)
    row_pick = ((~is_col)[..., None] & (pull[..., None] == shifts)).astype(jnp.float32)
    row_push = ((~is_col)[..., None] & (push[..., None] == shifts)).astype(jnp.float32)
    forward = []
    for height in range(levels):
        target = top_right[height] - updates[height]
        if height > 0:
            picked = gather_sources(forward[-1], col_pick[height - 1], row_pick[height - 1])
            target = target - jnp.einsum(
                "jrs,jts->rt", picked, top_blocks[height - 1], precision=highest
            )
        forward.append(apply_inverse(top_inverse[height], target))
    backward = [None] * levels
    current = apply_transpose(top_inverse[levels - 1], forward[levels - 1])
    backward[levels - 1] = current
    for height in range(levels - 2, -1, -1):
        pieces = jnp.einsum("rt,jts->jrs", current, top_blocks[height], precision=highest)
        incoming = push_back(pieces, col_pick[height], row_push[height])
        current = apply_transpose(top_inverse[height], forward[height] - incoming)
        backward[height] = current
    return jnp.stack(backward)


def on_device(local_inv, local_off, local_dep, local_rhs, top_inv, top_off, top_dep, top_rhs):
    inverse = local_inv[0, 0]
    blocks = local_off[0, 0]
    ancestor_levels = local_dep[0, 0]
    right_local = local_rhs[0, 0]
    levels = top_inv.shape[0]
    top_inverse = top_inv[:, 0, 0]
    top_blocks = top_off[:, 0, 0]
    top_links = top_dep[:, 0, 0]
    top_right = top_rhs[:, 0, 0]
    local_first = jnp.einsum("krs,kts->krt", right_local, inverse, precision=highest)
    contributions = jnp.einsum("krs,kjts->kjrt", local_first, blocks, precision=highest)
    level_matches = (ancestor_levels[:, :, None] == jnp.arange(levels, dtype=jnp.int32)).astype(
        jnp.float32
    )
    updates = jnp.einsum("kjl,kjrt->lrt", level_matches, contributions, precision=highest)
    n_leaf = lax.axis_size("leaf")
    by_shift = jnp.stack([updates] + [shifted(updates, "leaf", k) for k in range(1, n_leaf)])
    order = jnp.mod(lax.axis_index("leaf") - jnp.arange(n_leaf, dtype=jnp.int32), n_leaf)
    weights = (order[:, None] == jnp.arange(n_leaf, dtype=jnp.int32)).astype(jnp.float32)
    ordered = jnp.einsum("uk,klrs->ulrs", weights, by_shift, precision=highest)
    totals = ordered[0]
    for u in range(1, n_leaf):
        totals = totals + ordered[u]
    top_solution = solve_top(top_inverse, top_blocks, top_links, top_right, totals)
    ancestors = jnp.einsum("kjl,lrt->kjrt", level_matches, top_solution, precision=highest)
    remainder = local_first - jnp.einsum("kjrt,kjts->krs", ancestors, blocks, precision=highest)
    local_solution = jnp.einsum("krs,kst->krt", remainder, inverse, precision=highest)
    return (local_solution[None, None], top_solution[:, None, None])


def solution(mesh):
    placed = (
        P("leaf", "row", "col", None, None),
        P("leaf", "row", "col", None, None, None),
        P("leaf", "row", "col", None),
        P("leaf", "row", "col", None, None),
        P(None, "row", "col", None, None),
        P(None, "row", "col", None, None, None),
        P(None, "row", "col", None),
        P(None, "row", "col", None, None),
    )
    return jax.shard_map(
        on_device,
        mesh=mesh,
        in_specs=placed,
        out_specs=(P("leaf", "row", "col", None, None), P(None, "row", "col", None, None)),
        check_vma=False,
    )
```

```python
import jax
import jax.numpy as jnp
from jax import lax
from jax.sharding import PartitionSpec as P

highest = lax.Precision.HIGHEST


def apply_inverse(inverse, block):
    return jnp.einsum("rs,ts->rt", block, inverse, precision=highest)


def apply_transpose(inverse, block):
    return jnp.einsum("rs,st->rt", block, inverse, precision=highest)


def shifted(value, axis, k):
    n = lax.axis_size(axis)
    return lax.ppermute(value, axis, [(i, (i + k) % n) for i in range(n)])


def select_sum(mask, stacked):
    mask = mask.reshape(mask.shape + (1,) * (stacked.ndim - 1))
    return jnp.sum(jnp.where(mask, stacked[None], 0.0), axis=1)


def spread_sum(mask, pieces):
    return jnp.sum(jnp.where(mask[:, :, None, None], pieces[:, None], 0.0), axis=0)


def gather_sources(block, col_pick, row_pick):
    by_col = lax.all_gather(block[None], "col", axis=0, tiled=True)
    n_row = lax.axis_size("row")
    by_shift = jnp.stack([block] + [shifted(block, "row", k) for k in range(1, n_row)])
    return select_sum(col_pick, by_col) + select_sum(row_pick, by_shift)


def push_back(pieces, col_pick, row_push):
    n_row = lax.axis_size("row")
    slots = spread_sum(col_pick, pieces)
    incoming = lax.all_to_all(slots, "col", 0, 0, tiled=True).sum(0)
    parts = spread_sum(row_push, pieces)
    incoming = incoming + parts[0]
    for k in range(1, n_row):
        incoming = incoming + shifted(parts[k], "row", k)
    return incoming


def solve_top(top_inverse, top_blocks, top_links, top_right, updates):
    levels = top_inverse.shape[0]
    width_cols = lax.axis_size("col")
    n_row = lax.axis_size("row")
    me_row = lax.axis_index("row")
    is_col = top_links < width_cols
    col_pick = top_links[..., None] == jnp.arange(width_cols, dtype=jnp.int32)
    pull = jnp.mod(me_row - (top_links - width_cols), n_row)
    push = jnp.mod(top_links - width_cols - me_row, n_row)
    shifts = jnp.arange(n_row, dtype=jnp.int32)
    row_pick = (~is_col)[..., None] & (pull[..., None] == shifts)
    row_push = (~is_col)[..., None] & (push[..., None] == shifts)
    forward = []
    for height in range(levels):
        target = top_right[height] - updates[height]
        if height > 0:
            picked = gather_sources(forward[-1], col_pick[height - 1], row_pick[height - 1])
            target = target - jnp.einsum(
                "jrs,jts->rt", picked, top_blocks[height - 1], precision=highest
            )
        forward.append(apply_inverse(top_inverse[height], target))
    backward = [None] * levels
    current = apply_transpose(top_inverse[levels - 1], forward[levels - 1])
    backward[levels - 1] = current
    for height in range(levels - 2, -1, -1):
        pieces = jnp.einsum("rt,jts->jrs", current, top_blocks[height], precision=highest)
        incoming = push_back(pieces, col_pick[height], row_push[height])
        current = apply_transpose(top_inverse[height], forward[height] - incoming)
        backward[height] = current
    return jnp.stack(backward)


def on_device(local_inv, local_off, local_dep, local_rhs, top_inv, top_off, top_dep, top_rhs):
    inverse = local_inv[0, 0]
    blocks = local_off[0, 0]
    ancestor_levels = local_dep[0, 0]
    right_local = local_rhs[0, 0]
    levels = top_inv.shape[0]
    top_inverse = top_inv[:, 0, 0]
    top_blocks = top_off[:, 0, 0]
    top_links = top_dep[:, 0, 0]
    top_right = top_rhs[:, 0, 0]
    local_first = jnp.einsum("krs,kts->krt", right_local, inverse, precision=highest)
    contributions = jnp.einsum("krs,kjts->kjrt", local_first, blocks, precision=highest)
    level_matches = (ancestor_levels[:, :, None] == jnp.arange(levels, dtype=jnp.int32)).astype(
        jnp.float32
    )
    updates = jnp.einsum("kjl,kjrt->lrt", level_matches, contributions, precision=highest)
    n_leaf = lax.axis_size("leaf")
    by_shift = jnp.stack([updates] + [shifted(updates, "leaf", k) for k in range(1, n_leaf)])
    order = jnp.mod(lax.axis_index("leaf") - jnp.arange(n_leaf, dtype=jnp.int32), n_leaf)
    weights = order[:, None] == jnp.arange(n_leaf, dtype=jnp.int32)
    ordered = select_sum(weights, by_shift)
    totals = ordered[0]
    for u in range(1, n_leaf):
        totals = totals + ordered[u]
    top_solution = solve_top(top_inverse, top_blocks, top_links, top_right, totals)
    ancestors = jnp.einsum("kjl,lrt->kjrt", level_matches, top_solution, precision=highest)
    remainder = local_first - jnp.einsum("kjrt,kjts->krs", ancestors, blocks, precision=highest)
    local_solution = jnp.einsum("krs,kst->krt", remainder, inverse, precision=highest)
    return (local_solution[None, None], top_solution[:, None, None])


def solution(mesh):
    placed = (
        P("leaf", "row", "col", None, None),
        P("leaf", "row", "col", None, None, None),
        P("leaf", "row", "col", None),
        P("leaf", "row", "col", None, None),
        P(None, "row", "col", None, None),
        P(None, "row", "col", None, None, None),
        P(None, "row", "col", None),
        P(None, "row", "col", None, None),
    )
    return jax.shard_map(
        on_device,
        mesh=mesh,
        in_specs=placed,
        out_specs=(P("leaf", "row", "col", None, None), P(None, "row", "col", None, None)),
        check_vma=False,
    )
```

```python
import jax
import jax.numpy as jnp
from jax import lax
from jax.sharding import PartitionSpec as P

highest = lax.Precision.HIGHEST


def apply_inverse(inverse, block):
    return jnp.einsum("rs,ts->rt", block, inverse, precision=highest)


def apply_transpose(inverse, block):
    return jnp.einsum("rs,st->rt", block, inverse, precision=highest)


def shifted(value, axis, k):
    n = lax.axis_size(axis)
    return lax.ppermute(value, axis, [(i, (i + k) % n) for i in range(n)])


def select_sum(mask, stacked):
    mask = mask.reshape(mask.shape + (1,) * (stacked.ndim - 1))
    return jnp.sum(jnp.where(mask, stacked[None], 0.0), axis=1)


def spread_sum(mask, pieces):
    return jnp.sum(jnp.where(mask[:, :, None, None], pieces[:, None], 0.0), axis=0)


def gather_sources(block, col_pick, row_pick):
    by_col = lax.all_gather(block[None], "col", axis=0, tiled=True)
    n_row = lax.axis_size("row")
    by_shift = jnp.stack([block] + [shifted(block, "row", k) for k in range(1, n_row)])
    return select_sum(col_pick, by_col) + select_sum(row_pick, by_shift)


def push_back(pieces, col_pick, row_push):
    n_row = lax.axis_size("row")
    slots = spread_sum(col_pick, pieces)
    incoming = lax.all_to_all(slots, "col", 0, 0, tiled=True).sum(0)
    parts = spread_sum(row_push, pieces)
    incoming = incoming + parts[0]
    for k in range(1, n_row):
        incoming = incoming + shifted(parts[k], "row", k)
    return incoming


def solve_top(top_inverse, top_blocks, top_links, top_right, updates):
    levels = top_inverse.shape[0]
    width_cols = lax.axis_size("col")
    n_row = lax.axis_size("row")
    me_row = lax.axis_index("row")
    is_col = top_links < width_cols
    col_pick = top_links[..., None] == jnp.arange(width_cols, dtype=jnp.int32)
    pull = jnp.mod(me_row - (top_links - width_cols), n_row)
    push = jnp.mod(top_links - width_cols - me_row, n_row)
    shifts = jnp.arange(n_row, dtype=jnp.int32)
    row_pick = (~is_col)[..., None] & (pull[..., None] == shifts)
    row_push = (~is_col)[..., None] & (push[..., None] == shifts)
    forward = []
    for height in range(levels):
        target = top_right[height] - updates[height]
        if height > 0:
            picked = gather_sources(forward[-1], col_pick[height - 1], row_pick[height - 1])
            target = target - jnp.einsum(
                "jrs,jts->rt", picked, top_blocks[height - 1], precision=highest
            )
        forward.append(apply_inverse(top_inverse[height], target))
    backward = [None] * levels
    current = apply_transpose(top_inverse[levels - 1], forward[levels - 1])
    backward[levels - 1] = current
    for height in range(levels - 2, -1, -1):
        pieces = jnp.einsum("rt,jts->jrs", current, top_blocks[height], precision=highest)
        incoming = push_back(pieces, col_pick[height], row_push[height])
        current = apply_transpose(top_inverse[height], forward[height] - incoming)
        backward[height] = current
    return jnp.stack(backward)


def on_device(local_inv, local_off, local_dep, local_rhs, top_inv, top_off, top_dep, top_rhs):
    inverse = local_inv[0, 0]
    blocks = local_off[0, 0]
    ancestor_levels = local_dep[0, 0]
    right_local = local_rhs[0, 0]
    levels = top_inv.shape[0]
    top_inverse = top_inv[:, 0, 0]
    top_blocks = top_off[:, 0, 0]
    top_links = top_dep[:, 0, 0]
    top_right = top_rhs[:, 0, 0]
    local_first = jnp.einsum("krs,kts->krt", right_local, inverse, precision=highest)
    contributions = jnp.einsum("krs,kjts->kjrt", local_first, blocks, precision=highest)
    loc, fan = ancestor_levels.shape
    level_matches = (ancestor_levels.reshape(loc * fan)[:, None] == jnp.arange(levels, dtype=jnp.int32))
    updates = spread_sum(level_matches, contributions.reshape((loc * fan,) + contributions.shape[2:]))
    n_leaf = lax.axis_size("leaf")
    by_shift = jnp.stack([updates] + [shifted(updates, "leaf", k) for k in range(1, n_leaf)])
    order = jnp.mod(lax.axis_index("leaf") - jnp.arange(n_leaf, dtype=jnp.int32), n_leaf)
    weights = order[:, None] == jnp.arange(n_leaf, dtype=jnp.int32)
    ordered = select_sum(weights, by_shift)
    totals = ordered[0]
    for u in range(1, n_leaf):
        totals = totals + ordered[u]
    top_solution = solve_top(top_inverse, top_blocks, top_links, top_right, totals)
    ancestors = select_sum(level_matches, top_solution).reshape((loc, fan) + top_solution.shape[1:])
    remainder = local_first - jnp.einsum("kjrt,kjts->krs", ancestors, blocks, precision=highest)
    local_solution = jnp.einsum("krs,kst->krt", remainder, inverse, precision=highest)
    return (local_solution[None, None], top_solution[:, None, None])


def solution(mesh):
    placed = (
        P("leaf", "row", "col", None, None),
        P("leaf", "row", "col", None, None, None),
        P("leaf", "row", "col", None),
        P("leaf", "row", "col", None, None),
        P(None, "row", "col", None, None),
        P(None, "row", "col", None, None, None),
        P(None, "row", "col", None),
        P(None, "row", "col", None, None),
    )
    return jax.shard_map(
        on_device,
        mesh=mesh,
        in_specs=placed,
        out_specs=(P("leaf", "row", "col", None, None), P(None, "row", "col", None, None)),
        check_vma=False,
    )
```

```python
import jax
import jax.numpy as jnp
from jax import lax
from jax.sharding import PartitionSpec as P

highest = lax.Precision.HIGHEST


def apply_inverse(inverse, block):
    return jnp.einsum("rs,ts->rt", block, inverse, precision=highest)


def apply_transpose(inverse, block):
    return jnp.einsum("rs,st->rt", block, inverse, precision=highest)


def shifted(value, axis, k):
    n = lax.axis_size(axis)
    return lax.ppermute(value, axis, [(i, (i + k) % n) for i in range(n)])


def select_sum(mask, stacked):
    mask = mask.reshape(mask.shape + (1,) * (stacked.ndim - 1))
    return jnp.sum(jnp.where(mask, stacked[None], 0.0), axis=1)


def spread_sum(mask, pieces):
    return jnp.sum(jnp.where(mask[:, :, None, None], pieces[:, None], 0.0), axis=0)


def gather_sources(block, col_pick, row_pick):
    by_col = lax.all_gather(block[None], "col", axis=0, tiled=True)
    n_row = lax.axis_size("row")
    by_shift = jnp.stack([block] + [shifted(block, "row", k) for k in range(1, n_row)])
    return select_sum(col_pick, by_col) + select_sum(row_pick, by_shift)


def push_back(pieces, col_pick, row_push):
    n_row = lax.axis_size("row")
    slots = spread_sum(col_pick, pieces)
    incoming = lax.all_to_all(slots, "col", 0, 0, tiled=True).sum(0)
    parts = spread_sum(row_push, pieces)
    incoming = incoming + parts[0]
    for k in range(1, n_row):
        incoming = incoming + shifted(parts[k], "row", k)
    return incoming


def solve_top(top_inverse, top_blocks, top_links, top_right, updates):
    levels = top_inverse.shape[0]
    width_cols = lax.axis_size("col")
    n_row = lax.axis_size("row")
    me_row = lax.axis_index("row")
    is_col = top_links < width_cols
    col_pick = top_links[..., None] == jnp.arange(width_cols, dtype=jnp.int32)
    pull = jnp.mod(me_row - (top_links - width_cols), n_row)
    push = jnp.mod(top_links - width_cols - me_row, n_row)
    shifts = jnp.arange(n_row, dtype=jnp.int32)
    row_pick = (~is_col)[..., None] & (pull[..., None] == shifts)
    row_push = (~is_col)[..., None] & (push[..., None] == shifts)
    forward = []
    for height in range(levels):
        target = top_right[height] - updates[height]
        if height > 0:
            picked = gather_sources(forward[-1], col_pick[height - 1], row_pick[height - 1])
            target = target - jnp.einsum(
                "jrs,jts->rt", picked, top_blocks[height - 1], precision=highest
            )
        forward.append(apply_inverse(top_inverse[height], target))
    forward = jnp.stack(forward)
    current = apply_transpose(top_inverse[levels - 1], forward[levels - 1])
    solved = jnp.zeros_like(forward).at[levels - 1].set(current)

    def step(i, carry):
        current, solved = carry
        height = levels - 2 - i
        at = lambda a: lax.dynamic_index_in_dim(a, height, 0, keepdims=False)
        pieces = jnp.einsum("rt,jts->jrs", current, at(top_blocks), precision=highest)
        incoming = push_back(pieces, at(col_pick), at(row_push))
        current = apply_transpose(at(top_inverse), at(forward) - incoming)
        return current, lax.dynamic_update_index_in_dim(solved, current, height, 0)

    return lax.fori_loop(0, levels - 1, step, (current, solved))[1]


def on_device(local_inv, local_off, local_dep, local_rhs, top_inv, top_off, top_dep, top_rhs):
    inverse = local_inv[0, 0]
    blocks = local_off[0, 0]
    ancestor_levels = local_dep[0, 0]
    right_local = local_rhs[0, 0]
    levels = top_inv.shape[0]
    top_inverse = top_inv[:, 0, 0]
    top_blocks = top_off[:, 0, 0]
    top_links = top_dep[:, 0, 0]
    top_right = top_rhs[:, 0, 0]
    local_first = jnp.einsum("krs,kts->krt", right_local, inverse, precision=highest)
    contributions = jnp.einsum("krs,kjts->kjrt", local_first, blocks, precision=highest)
    level_matches = (ancestor_levels[:, :, None] == jnp.arange(levels, dtype=jnp.int32)).astype(
        jnp.float32
    )
    updates = jnp.einsum("kjl,kjrt->lrt", level_matches, contributions, precision=highest)
    n_leaf = lax.axis_size("leaf")
    by_shift = jnp.stack([updates] + [shifted(updates, "leaf", k) for k in range(1, n_leaf)])
    order = jnp.mod(lax.axis_index("leaf") - jnp.arange(n_leaf, dtype=jnp.int32), n_leaf)
    weights = order[:, None] == jnp.arange(n_leaf, dtype=jnp.int32)
    ordered = select_sum(weights, by_shift)
    totals = ordered[0]
    for u in range(1, n_leaf):
        totals = totals + ordered[u]
    top_solution = solve_top(top_inverse, top_blocks, top_links, top_right, totals)
    ancestors = jnp.einsum("kjl,lrt->kjrt", level_matches, top_solution, precision=highest)
    remainder = local_first - jnp.einsum("kjrt,kjts->krs", ancestors, blocks, precision=highest)
    local_solution = jnp.einsum("krs,kst->krt", remainder, inverse, precision=highest)
    return (local_solution[None, None], top_solution[:, None, None])


def solution(mesh):
    placed = (
        P("leaf", "row", "col", None, None),
        P("leaf", "row", "col", None, None, None),
        P("leaf", "row", "col", None),
        P("leaf", "row", "col", None, None),
        P(None, "row", "col", None, None),
        P(None, "row", "col", None, None, None),
        P(None, "row", "col", None),
        P(None, "row", "col", None, None),
    )
    return jax.shard_map(
        on_device,
        mesh=mesh,
        in_specs=placed,
        out_specs=(P("leaf", "row", "col", None, None), P(None, "row", "col", None, None)),
        check_vma=False,
    )
```

```python
import jax
import jax.numpy as jnp
from jax import lax
from jax.sharding import PartitionSpec as P

highest = lax.Precision.HIGHEST


def apply_inverse(inverse, block):
    return jnp.einsum("rs,ts->rt", block, inverse, precision=highest)


def apply_transpose(inverse, block):
    return jnp.einsum("rs,st->rt", block, inverse, precision=highest)


def shifted(value, axis, k):
    n = lax.axis_size(axis)
    return lax.ppermute(value, axis, [(i, (i + k) % n) for i in range(n)])


def select_sum(mask, stacked):
    mask = mask.reshape(mask.shape + (1,) * (stacked.ndim - 1))
    return jnp.sum(jnp.where(mask, stacked[None], 0.0), axis=1)


def spread_sum(mask, pieces):
    return jnp.sum(jnp.where(mask[:, :, None, None], pieces[:, None], 0.0), axis=0)


def gather_sources(block, col_pick, row_pick):
    by_col = lax.all_gather(block[None], "col", axis=0, tiled=True)
    n_row = lax.axis_size("row")
    by_shift = jnp.stack([block] + [shifted(block, "row", k) for k in range(1, n_row)])
    return select_sum(col_pick, by_col) + select_sum(row_pick, by_shift)


def push_back(pieces, col_pick, row_push):
    n_row = lax.axis_size("row")
    slots = spread_sum(col_pick, pieces)
    incoming = lax.all_to_all(slots, "col", 0, 0, tiled=True).sum(0)
    parts = spread_sum(row_push, pieces)
    incoming = incoming + parts[0]
    for k in range(1, n_row):
        incoming = incoming + shifted(parts[k], "row", k)
    return incoming


def solve_top(top_inverse, top_blocks, top_links, top_right, updates):
    levels = top_inverse.shape[0]
    width_cols = lax.axis_size("col")
    n_row = lax.axis_size("row")
    me_row = lax.axis_index("row")
    is_col = top_links < width_cols
    col_pick = top_links[..., None] == jnp.arange(width_cols, dtype=jnp.int32)
    pull = jnp.mod(me_row - (top_links - width_cols), n_row)
    push = jnp.mod(top_links - width_cols - me_row, n_row)
    shifts = jnp.arange(n_row, dtype=jnp.int32)
    row_pick = (~is_col)[..., None] & (pull[..., None] == shifts)
    row_push = (~is_col)[..., None] & (push[..., None] == shifts)
    first = apply_inverse(top_inverse[0], top_right[0] - updates[0])
    forward = jnp.zeros_like(updates).at[0].set(first)

    def down(height, carry):
        latest, forward = carry
        at = lambda a: lax.dynamic_index_in_dim(a, height, 0, keepdims=False)
        below = lambda a: lax.dynamic_index_in_dim(a, height - 1, 0, keepdims=False)
        picked = gather_sources(latest, below(col_pick), below(row_pick))
        target = at(top_right) - at(updates)
        target = target - jnp.einsum("jrs,jts->rt", picked, below(top_blocks), precision=highest)
        latest = apply_inverse(at(top_inverse), target)
        return latest, lax.dynamic_update_index_in_dim(forward, latest, height, 0)

    forward = lax.fori_loop(1, levels, down, (first, forward))[1]
    current = apply_transpose(top_inverse[levels - 1], forward[levels - 1])
    solved = jnp.zeros_like(forward).at[levels - 1].set(current)

    def step(i, carry):
        current, solved = carry
        height = levels - 2 - i
        at = lambda a: lax.dynamic_index_in_dim(a, height, 0, keepdims=False)
        pieces = jnp.einsum("rt,jts->jrs", current, at(top_blocks), precision=highest)
        incoming = push_back(pieces, at(col_pick), at(row_push))
        current = apply_transpose(at(top_inverse), at(forward) - incoming)
        return current, lax.dynamic_update_index_in_dim(solved, current, height, 0)

    return lax.fori_loop(0, levels - 1, step, (current, solved))[1]


def on_device(local_inv, local_off, local_dep, local_rhs, top_inv, top_off, top_dep, top_rhs):
    inverse = local_inv[0, 0]
    blocks = local_off[0, 0]
    ancestor_levels = local_dep[0, 0]
    right_local = local_rhs[0, 0]
    levels = top_inv.shape[0]
    top_inverse = top_inv[:, 0, 0]
    top_blocks = top_off[:, 0, 0]
    top_links = top_dep[:, 0, 0]
    top_right = top_rhs[:, 0, 0]
    local_first = jnp.einsum("krs,kts->krt", right_local, inverse, precision=highest)
    contributions = jnp.einsum("krs,kjts->kjrt", local_first, blocks, precision=highest)
    level_matches = (ancestor_levels[:, :, None] == jnp.arange(levels, dtype=jnp.int32)).astype(
        jnp.float32
    )
    updates = jnp.einsum("kjl,kjrt->lrt", level_matches, contributions, precision=highest)
    n_leaf = lax.axis_size("leaf")
    by_shift = jnp.stack([updates] + [shifted(updates, "leaf", k) for k in range(1, n_leaf)])
    order = jnp.mod(lax.axis_index("leaf") - jnp.arange(n_leaf, dtype=jnp.int32), n_leaf)
    weights = order[:, None] == jnp.arange(n_leaf, dtype=jnp.int32)
    ordered = select_sum(weights, by_shift)
    totals = ordered[0]
    for u in range(1, n_leaf):
        totals = totals + ordered[u]
    top_solution = solve_top(top_inverse, top_blocks, top_links, top_right, totals)
    ancestors = jnp.einsum("kjl,lrt->kjrt", level_matches, top_solution, precision=highest)
    remainder = local_first - jnp.einsum("kjrt,kjts->krs", ancestors, blocks, precision=highest)
    local_solution = jnp.einsum("krs,kst->krt", remainder, inverse, precision=highest)
    return (local_solution[None, None], top_solution[:, None, None])


def solution(mesh):
    placed = (
        P("leaf", "row", "col", None, None),
        P("leaf", "row", "col", None, None, None),
        P("leaf", "row", "col", None),
        P("leaf", "row", "col", None, None),
        P(None, "row", "col", None, None),
        P(None, "row", "col", None, None, None),
        P(None, "row", "col", None),
        P(None, "row", "col", None, None),
    )
    return jax.shard_map(
        on_device,
        mesh=mesh,
        in_specs=placed,
        out_specs=(P("leaf", "row", "col", None, None), P(None, "row", "col", None, None)),
        check_vma=False,
    )
```
